256 devices in a mesh: patch: 8 (over z), tm: 8 (over y, core), subject: 4 (over x).
Axes of the slice: x: 4, y: 4, z: 8, core: 2. Of those that a mesh axis runs over, the one named last changes fastest.
Arguments:
- frames_in: bfloat16 [256, 512, 512], P(('subject', 'patch', 'tm')), parts along dimension 0, may hold values from -6 to 6
- spatial_qkv: bfloat16 [512, 1536], replicated, may hold values from -20 to 20, as said below
- spatial_out: bfloat16 [512, 512], replicated, may hold values from -0.25 to 0.25
- temporal_qkv: bfloat16 [512, 1536], replicated, may hold values from -20 to 20, as said below
- temporal_out: bfloat16 [512, 512], replicated, may hold values from -0.25 to 0.25
Outputs:
- frames_out: bfloat16 [256, 512, 512], P(('subject', 'patch', 'tm')), parts along dimension 0
The draws below stay inside these ranges and needn't reach their ends.
There are 4 independent parts, one for each index of `subject`. The reference program is written for one: setup_inputs(seed, part) draws one part's arguments, and reference() takes and returns one part's arrays. A program takes and returns all parts, laid end to end along the dimension named above; an argument that names none is the same for every part. Nothing has to cross between parts.
Inputs may be any that keep to these rules, and one draw needn't show every extreme that they name: `spatial_qkv`: columns hold query, key and value projections in that order, each 8 heads of 64. `temporal_qkv`: columns hold query, key and value projections in that order, each 8 heads of 64.
All inputs are finite; a program needn't handle non-finite values.
Results may differ from the reference program's by a relative error of at most 0.015.
Values may be sent and summed in bfloat16 or wider, within the bound.
No kernel may reach another device: no remote copies, remote signals or barrier semaphores. Data moves between devices by JAX's collectives and lax.ppermute only.
A program may use at most 64 MiB of HBM per device.

```python
import jax
import jax.numpy as jnp
from jax import lax

D = 512
HEADS = 8
PATCHES = 512
FRAMES = 64


def qkv_table(key):
    split_query, split_keys, split_values = jax.random.split(key, 3)
    spread = D ** (-0.5)
    queries = jax.random.normal(split_query, (D, D), jnp.float32) * (1.4 * spread)
    key_part = jax.random.normal(split_keys, (D, D), jnp.float32) * (1.4 * spread)
    value_part = jax.random.normal(split_values, (D, D), jnp.float32) * (2.0 * spread)
    return jnp.concatenate([queries, key_part, value_part], axis=1)


def draw_spatial_qkv(key, part):
    return qkv_table(jax.random.fold_in(key, 11)).astype(jnp.bfloat16)


def draw_temporal_qkv(key, part):
    return qkv_table(jax.random.fold_in(key, 23)).astype(jnp.bfloat16)


def levels(own_key, shape, cuts, low, high):
    def one(dim, blocks):
        draws = jax.random.uniform(jax.random.fold_in(jax.random.fold_in(own_key, 6), dim), (blocks,), jnp.float32, low / len(cuts), high / len(cuts))
        return jnp.repeat(jnp.exp(draws), shape[dim] // blocks).reshape((-1,) + (1,) * (len(shape) - dim - 1))

    factor_of = one(*cuts[0])
    for cut in cuts[1:]:
        factor_of = factor_of * one(*cut)
    return factor_of


def normal_values(rng, dims, width, bound, shards=(), held_as=jnp.bfloat16):
    values = jax.random.normal(rng, dims, jnp.float32) * width
    if len(shards) > 0:
        values = levels(rng, dims, shards, -0.22, 0.18) * values
    return jnp.clip(values, min=-bound, max=bound).astype(held_as)


def setup_inputs(seed: int = 0, part: int = 0) -> dict:
    seeds = jax.random.split(jax.random.key(seed), 6)
    own_keys = jax.random.split(jax.random.fold_in(seeds[5], part), 6)
    return {
        "frames_in": normal_values(own_keys[0], (FRAMES, PATCHES, D), 1.0, 6.0, ((0, 64),)),
        "spatial_qkv": draw_spatial_qkv(jax.random.fold_in(seeds[5], 71), part),
        "spatial_out": normal_values(seeds[2], (D, D), D ** -0.5, 0.25),
        "temporal_qkv": draw_temporal_qkv(jax.random.fold_in(seeds[5], 71), part),
        "temporal_out": normal_values(seeds[4], (D, D), D ** -0.5, 0.25),
    }


epsilon = 1e-05
floor_score = -1e+30

def layer_norm(input_rows):
    as_float = input_rows.astype(jnp.float32)
    centre = lax.optimization_barrier(jnp.mean(as_float, axis=-1, keepdims=True))
    centered = as_float - centre
    spread = lax.optimization_barrier(jnp.mean(centered * centered, axis=-1, keepdims=True))
    return (centered * lax.rsqrt(spread + epsilon)).astype(jnp.bfloat16)

def project_heads(input_rows, qkv_weight):
    model_width = input_rows.shape[-1]
    normed = layer_norm(input_rows)
    packed = jnp.dot(normed.reshape(-1, model_width), qkv_weight, preferred_element_type=jnp.float32).astype(jnp.bfloat16)
    packed = lax.optimization_barrier(packed).astype(jnp.float32)
    shaped = packed.reshape(input_rows.shape[:-1] + (3, HEADS, model_width // HEADS))
    return (shaped[..., 0, :, :], shaped[..., 1, :, :], shaped[..., 2, :, :])

def spatial_frame(one_frame, qkv_weight, out_weight):
    queries, key_rows, value_rows = project_heads(one_frame, qkv_weight)
    factor = queries.shape[-1] ** (-0.5)
    scores = jnp.einsum('qhd,khd->hqk', queries, key_rows) * factor
    highest = lax.optimization_barrier(jnp.max(scores, axis=-1, keepdims=True))
    exp_terms = jnp.exp(scores - highest)
    row_total = lax.optimization_barrier(jnp.sum(exp_terms, axis=-1))
    weights = lax.optimization_barrier(exp_terms.astype(jnp.bfloat16)).astype(jnp.float32)
    mixture = jnp.einsum('hqk,khd->qhd', weights, value_rows)
    mixture = (mixture / jnp.transpose(row_total)[:, :, None]).astype(jnp.bfloat16)
    update = jnp.dot(mixture.reshape(one_frame.shape), out_weight, preferred_element_type=jnp.float32)
    return (one_frame.astype(jnp.float32) + update).astype(jnp.bfloat16)

def causal_columns(columns, qkv_weight, out_weight):
    queries, key_rows, value_rows = project_heads(columns, qkv_weight)
    factor = queries.shape[-1] ** (-0.5)
    scores = jnp.einsum('qchd,kchd->chqk', queries, key_rows) * factor
    frame_order = jnp.arange(columns.shape[0], dtype=jnp.int32)
    allowed = frame_order[None, :] <= frame_order[:, None]
    masked = jnp.where(allowed, scores, floor_score)
    highest = lax.optimization_barrier(jnp.max(masked, axis=-1, keepdims=True))
    exp_terms = jnp.where(allowed, jnp.exp(masked - highest), 0.0)
    row_total = lax.optimization_barrier(jnp.sum(exp_terms, axis=-1))
    weights = lax.optimization_barrier(exp_terms.astype(jnp.bfloat16)).astype(jnp.float32)
    mixture = jnp.einsum('chqk,kchd->qchd', weights, value_rows)
    mixture = (mixture / jnp.transpose(row_total, (2, 0, 1))[..., None]).astype(jnp.bfloat16)
    model_width = columns.shape[-1]
    update = jnp.dot(mixture.reshape(-1, model_width), out_weight, preferred_element_type=jnp.float32)
    return (columns.astype(jnp.float32) + update.reshape(columns.shape)).astype(jnp.bfloat16)

def reference(frames_in, spatial_qkv, spatial_out, temporal_qkv, temporal_out):

    def frame_step(one_frame):
        return spatial_frame(one_frame, spatial_qkv, spatial_out)
    hidden = lax.map(frame_step, frames_in)
    group_size = 8
    grouped = hidden.reshape(FRAMES, PATCHES // group_size, group_size, D).transpose(1, 0, 2, 3)

    def group_step(columns):
        return causal_columns(columns, temporal_qkv, temporal_out)
    result = lax.map(group_step, grouped)
    return result.transpose(1, 0, 2, 3).reshape(FRAMES, PATCHES, D)
```

```python
import jax
import jax.numpy as jnp
from jax import lax
from jax.experimental import pallas as pl
from jax.experimental.pallas import tpu as pltpu
from jax.sharding import PartitionSpec as P

HEADS = 8

epsilon = 1e-05
floor_score = -1e30


def _layer_norm(rows):
    width = rows.shape[-1]
    centre = jnp.sum(rows, axis=-1, keepdims=True) * (1.0 / width)
    centered = rows - centre
    spread = jnp.sum(centered * centered, axis=-1, keepdims=True) * (1.0 / width)
    return (centered * lax.rsqrt(spread + epsilon)).astype(jnp.bfloat16)


def _attention_block(x_ref, wqkv_ref, wout_ref, o_ref, packed_ref, attn_ref, mask_fn):
    rows = x_ref[...].astype(jnp.float32)
    width = rows.shape[-1]
    head_dim = width // HEADS
    normed = _layer_norm(rows)
    packed_ref[...] = jnp.dot(
        normed, wqkv_ref[...], preferred_element_type=jnp.float32
    ).astype(jnp.bfloat16)
    factor = head_dim ** (-0.5)
    n_rows = rows.shape[0]
    allowed = mask_fn(n_rows)
    lane = lax.broadcasted_iota(jnp.int32, (1, 2 * head_dim), 1)
    low = lane < head_dim
    for pair in range(HEADS // 2):
        cols = slice(pair * 2 * head_dim, (pair + 1) * 2 * head_dim)
        q2 = packed_ref[:, cols]
        k2 = packed_ref[:, width + cols.start : width + cols.stop]
        v2 = packed_ref[:, 2 * width + cols.start : 2 * width + cols.stop]
        halves = []
        for sel in (low, jnp.logical_not(low)):
            qh = jnp.where(sel, q2, jnp.zeros_like(q2))
            scores = (
                lax.dot_general(
                    qh, k2, (((1,), (1,)), ((), ())), preferred_element_type=jnp.float32
                )
                * factor
            )
            if allowed is not None:
                scores = jnp.where(allowed, scores, floor_score)
            highest = jnp.max(scores, axis=-1, keepdims=True)
            exp_terms = jnp.exp(scores - highest)
            if allowed is not None:
                exp_terms = jnp.where(allowed, exp_terms, 0.0)
            total = jnp.sum(exp_terms, axis=-1, keepdims=True)
            mixture = jnp.dot(
                exp_terms.astype(jnp.bfloat16), v2, preferred_element_type=jnp.float32
            )
            halves.append(mixture / total)
        attn_ref[:, cols] = jnp.where(low, halves[0], halves[1]).astype(jnp.bfloat16)
    update = jnp.dot(attn_ref[...], wout_ref[...], preferred_element_type=jnp.float32)
    o_ref[...] = (rows + update).astype(jnp.bfloat16)


def _no_mask(n_rows):
    return None


def _make_causal_mask(group):
    def mask_fn(n_rows):
        r_a = lax.broadcasted_iota(jnp.int32, (n_rows, n_rows), 0)
        r_b = lax.broadcasted_iota(jnp.int32, (n_rows, n_rows), 1)
        return (r_b <= r_a) & (jnp.bitwise_and(r_a - r_b, group - 1) == 0)

    return mask_fn


def _layer_call(rows, qkv_weight, out_weight, mask_fn):
    n_rows, width = rows.shape

    def kernel(x_ref, wqkv_ref, wout_ref, o_ref, packed_ref, attn_ref):
        _attention_block(x_ref, wqkv_ref, wout_ref, o_ref, packed_ref, attn_ref, mask_fn)

    vmem = pl.BlockSpec(memory_space=pltpu.VMEM)
    return pl.pallas_call(
        kernel,
        out_shape=jax.ShapeDtypeStruct((n_rows, width), jnp.bfloat16),
        in_specs=[vmem, vmem, vmem],
        out_specs=vmem,
        scratch_shapes=[
            pltpu.VMEM((n_rows, 3 * width), jnp.bfloat16),
            pltpu.VMEM((n_rows, width), jnp.bfloat16),
        ],
        compiler_params=pltpu.CompilerParams(vmem_limit_bytes=48 * 1024 * 1024),
    )(rows, qkv_weight, out_weight)


def body(frames_in, spatial_qkv, spatial_out, temporal_qkv, temporal_out):
    n_frames, n_patches, width = frames_in.shape
    hidden = jnp.stack(
        [_layer_call(frames_in[f], spatial_qkv, spatial_out, _no_mask) for f in range(n_frames)]
    )
    columns = lax.all_to_all(hidden, ("patch", "tm"), split_axis=1, concat_axis=0, tiled=True)
    frame_total, column_count, _ = columns.shape
    assert column_count & (column_count - 1) == 0
    result = _layer_call(
        columns.reshape(frame_total * column_count, width),
        temporal_qkv,
        temporal_out,
        _make_causal_mask(column_count),
    ).reshape(frame_total, column_count, width)
    return lax.all_to_all(result, ("patch", "tm"), split_axis=0, concat_axis=1, tiled=True)


def solution(mesh):
    in_specs = (P(("subject", "patch", "tm"), None, None), P(), P(), P(), P())
    out_specs = P(("subject", "patch", "tm"), None, None)
    return jax.shard_map(body, mesh=mesh, in_specs=in_specs, out_specs=out_specs, check_vma=False)
```

```python
import jax
import jax.numpy as jnp
from jax import lax
from jax.experimental import pallas as pl
from jax.experimental.pallas import tpu as pltpu
from jax.sharding import PartitionSpec as P

HEADS = 8

epsilon = 1e-05
floor_score = -1e30


def _layer_norm(rows):
    width = rows.shape[-1]
    centre = jnp.sum(rows, axis=-1, keepdims=True) * (1.0 / width)
    centered = rows - centre
    spread = jnp.sum(centered * centered, axis=-1, keepdims=True) * (1.0 / width)
    return (centered * lax.rsqrt(spread + epsilon)).astype(jnp.bfloat16)


def _attention_block(x_ref, wqkv_ref, wout_ref, o_ref, packed_ref, attn_ref, mask_fn):
    rows = x_ref[...].astype(jnp.float32)
    width = rows.shape[-1]
    head_dim = width // HEADS
    normed = _layer_norm(rows)
    packed_ref[...] = jnp.dot(
        normed, wqkv_ref[...], preferred_element_type=jnp.float32
    ).astype(jnp.bfloat16)
    factor = head_dim ** (-0.5)
    n_rows = rows.shape[0]
    allowed = mask_fn(n_rows)
    lane = lax.broadcasted_iota(jnp.int32, (1, 2 * head_dim), 1)
    low = lane < head_dim
    for pair in range(HEADS // 2):
        cols = slice(pair * 2 * head_dim, (pair + 1) * 2 * head_dim)
        q2 = packed_ref[:, cols]
        k2 = packed_ref[:, width + cols.start : width + cols.stop]
        v2 = packed_ref[:, 2 * width + cols.start : 2 * width + cols.stop]
        halves = []
        for sel in (low, jnp.logical_not(low)):
            qh = jnp.where(sel, q2, jnp.zeros_like(q2))
            scores = (
                lax.dot_general(
                    qh, k2, (((1,), (1,)), ((), ())), preferred_element_type=jnp.float32
                )
                * factor
            )
            if allowed is not None:
                scores = jnp.where(allowed, scores, floor_score)
            highest = jnp.max(scores, axis=-1, keepdims=True)
            exp_terms = jnp.exp(scores - highest)
            if allowed is not None:
                exp_terms = jnp.where(allowed, exp_terms, 0.0)
            total = jnp.sum(exp_terms, axis=-1, keepdims=True)
            mixture = jnp.dot(
                exp_terms.astype(jnp.bfloat16), v2, preferred_element_type=jnp.float32
            )
            halves.append(mixture / total)
        attn_ref[:, cols] = jnp.where(low, halves[0], halves[1]).astype(jnp.bfloat16)
    update = jnp.dot(attn_ref[...], wout_ref[...], preferred_element_type=jnp.float32)
    o_ref[...] = (rows + update).astype(jnp.bfloat16)


def _no_mask(n_rows):
    return None


def _make_causal_mask(group):
    def mask_fn(n_rows):
        r_a = lax.broadcasted_iota(jnp.int32, (n_rows, n_rows), 0)
        r_b = lax.broadcasted_iota(jnp.int32, (n_rows, n_rows), 1)
        return (r_b <= r_a) & (jnp.bitwise_and(r_a - r_b, group - 1) == 0)

    return mask_fn


def _layer_call(rows, qkv_weight, out_weight, mask_fn):
    n_rows, width = rows.shape

    def kernel(x_ref, wqkv_ref, wout_ref, o_ref, packed_ref, attn_ref):
        _attention_block(x_ref, wqkv_ref, wout_ref, o_ref, packed_ref, attn_ref, mask_fn)

    vmem = pl.BlockSpec(memory_space=pltpu.VMEM)
    return pl.pallas_call(
        kernel,
        out_shape=jax.ShapeDtypeStruct((n_rows, width), jnp.bfloat16),
        in_specs=[vmem, vmem, vmem],
        out_specs=vmem,
        scratch_shapes=[
            pltpu.VMEM((n_rows, 3 * width), jnp.bfloat16),
            pltpu.VMEM((n_rows, width), jnp.bfloat16),
        ],
        compiler_params=pltpu.CompilerParams(vmem_limit_bytes=48 * 1024 * 1024),
    )(rows, qkv_weight, out_weight)


def body(frames_in, spatial_qkv, spatial_out, temporal_qkv, temporal_out):
    n_frames, n_patches, width = frames_in.shape
    assert n_frames == 1
    group = lax.axis_size(("patch", "tm"))
    hidden = _layer_call(frames_in[0], spatial_qkv, spatial_out, _no_mask)
    columns = lax.all_to_all(
        hidden.reshape(group, n_patches // group, width),
        ("patch", "tm"),
        split_axis=0,
        concat_axis=0,
        tiled=True,
    )
    frame_total, column_count, _ = columns.shape
    assert column_count & (column_count - 1) == 0
    result = _layer_call(
        columns.reshape(frame_total * column_count, width),
        temporal_qkv,
        temporal_out,
        _make_causal_mask(column_count),
    ).reshape(frame_total, column_count, width)
    return lax.all_to_all(result, ("patch", "tm"), split_axis=0, concat_axis=1, tiled=True)


def solution(mesh):
    in_specs = (P(("subject", "patch", "tm"), None, None), P(), P(), P(), P())
    out_specs = P(("subject", "patch", "tm"), None, None)
    return jax.shard_map(body, mesh=mesh, in_specs=in_specs, out_specs=out_specs, check_vma=False)
```

```python
import jax
import jax.numpy as jnp
from jax import lax
from jax.experimental import pallas as pl
from jax.experimental.pallas import tpu as pltpu
from jax.sharding import PartitionSpec as P

HEADS = 8

epsilon = 1e-05
floor_score = -1e30


def _layer_norm(rows):
    width = rows.shape[-1]
    centre = jnp.sum(rows, axis=-1, keepdims=True) * (1.0 / width)
    centered = rows - centre
    spread = jnp.sum(centered * centered, axis=-1, keepdims=True) * (1.0 / width)
    return (centered * lax.rsqrt(spread + epsilon)).astype(jnp.bfloat16)


def _attention_block(x_ref, w_copies, wqkv_ref, wout_ref, o_ref, packed_ref, attn_ref, mask_fn):
    rows = x_ref[...].astype(jnp.float32)
    width = rows.shape[-1]
    head_dim = width // HEADS
    normed = _layer_norm(rows)
    for part in range(3):
        w_copies[part].wait()
        cols = slice(part * width, (part + 1) * width)
        packed_ref[:, cols] = jnp.dot(
            normed, wqkv_ref[:, cols], preferred_element_type=jnp.float32
        ).astype(jnp.bfloat16)
    factor = head_dim ** (-0.5)
    n_rows = rows.shape[0]
    allowed = mask_fn(n_rows)
    lane = lax.broadcasted_iota(jnp.int32, (1, 2 * head_dim), 1)
    low = lane < head_dim
    for pair in range(HEADS // 2):
        cols = slice(pair * 2 * head_dim, (pair + 1) * 2 * head_dim)
        q2 = packed_ref[:, cols]
        k2 = packed_ref[:, width + cols.start : width + cols.stop]
        v2 = packed_ref[:, 2 * width + cols.start : 2 * width + cols.stop]
        halves = []
        for sel in (low, jnp.logical_not(low)):
            qh = jnp.where(sel, q2, jnp.zeros_like(q2))
            scores = (
                lax.dot_general(
                    qh, k2, (((1,), (1,)), ((), ())), preferred_element_type=jnp.float32
                )
                * factor
            )
            if allowed is not None:
                scores = jnp.where(allowed, scores, floor_score)
            highest = jnp.max(scores, axis=-1, keepdims=True)
            exp_terms = jnp.exp(scores - highest)
            if allowed is not None:
                exp_terms = jnp.where(allowed, exp_terms, 0.0)
            total = jnp.sum(exp_terms, axis=-1, keepdims=True)
            mixture = jnp.dot(
                exp_terms.astype(jnp.bfloat16), v2, preferred_element_type=jnp.float32
            )
            halves.append(mixture / total)
        attn_ref[:, cols] = jnp.where(low, halves[0], halves[1]).astype(jnp.bfloat16)
    w_copies[3].wait()
    update = jnp.dot(attn_ref[...], wout_ref[...], preferred_element_type=jnp.float32)
    o_ref[...] = (rows + update).astype(jnp.bfloat16)


def _no_mask(n_rows):
    return None


def _make_causal_mask(group):
    def mask_fn(n_rows):
        r_a = lax.broadcasted_iota(jnp.int32, (n_rows, n_rows), 0)
        r_b = lax.broadcasted_iota(jnp.int32, (n_rows, n_rows), 1)
        return (r_b <= r_a) & (jnp.bitwise_and(r_a - r_b, group - 1) == 0)

    return mask_fn


def _layer_call(rows, qkv_weight, out_weight, mask_fn, rows_in_hbm):
    n_rows, width = rows.shape

    def kernel(x_in, wqkv_hbm, wout_hbm, o_ref, x_vmem, wqkv_ref, wout_ref, packed_ref, attn_ref, sems):
        if rows_in_hbm:
            x_copy = pltpu.make_async_copy(x_in, x_vmem, sems.at[4])
            x_copy.start()
        w_copies = [
            pltpu.make_async_copy(
                wqkv_hbm.at[:, pl.ds(part * width, width)],
                wqkv_ref.at[:, pl.ds(part * width, width)],
                sems.at[part],
            )
            for part in range(3)
        ]
        w_copies.append(pltpu.make_async_copy(wout_hbm, wout_ref, sems.at[3]))
        for copy in w_copies:
            copy.start()
        if rows_in_hbm:
            x_copy.wait()
            x_ref = x_vmem
        else:
            x_ref = x_in
        _attention_block(x_ref, w_copies, wqkv_ref, wout_ref, o_ref, packed_ref, attn_ref, mask_fn)

    vmem = pl.BlockSpec(memory_space=pltpu.VMEM)
    hbm = pl.BlockSpec(memory_space=pltpu.HBM)
    return pl.pallas_call(
        kernel,
        out_shape=jax.ShapeDtypeStruct((n_rows, width), jnp.bfloat16),
        in_specs=[hbm if rows_in_hbm else vmem, hbm, hbm],
        out_specs=vmem,
        scratch_shapes=[
            pltpu.VMEM((n_rows, width), jnp.bfloat16),
            pltpu.VMEM((width, 3 * width), jnp.bfloat16),
            pltpu.VMEM((width, width), jnp.bfloat16),
            pltpu.VMEM((n_rows, 3 * width), jnp.bfloat16),
            pltpu.VMEM((n_rows, width), jnp.bfloat16),
            pltpu.SemaphoreType.DMA((5,)),
        ],
        compiler_params=pltpu.CompilerParams(vmem_limit_bytes=48 * 1024 * 1024),
    )(
        pltpu.with_memory_space_constraint(rows, pltpu.HBM) if rows_in_hbm else rows,
        pltpu.with_memory_space_constraint(qkv_weight, pltpu.HBM),
        pltpu.with_memory_space_constraint(out_weight, pltpu.HBM),
    )


def body(frames_in, spatial_qkv, spatial_out, temporal_qkv, temporal_out):
    n_frames, n_patches, width = frames_in.shape
    assert n_frames == 1
    group = lax.axis_size(("patch", "tm"))
    hidden = _layer_call(frames_in[0], spatial_qkv, spatial_out, _no_mask, True)
    columns = lax.all_to_all(
        hidden.reshape(group, n_patches // group, width),
        ("patch", "tm"),
        split_axis=0,
        concat_axis=0,
        tiled=True,
    )
    frame_total, column_count, _ = columns.shape
    assert column_count & (column_count - 1) == 0
    result = _layer_call(
        columns.reshape(frame_total * column_count, width),
        temporal_qkv,
        temporal_out,
        _make_causal_mask(column_count),
        False,
    ).reshape(frame_total, column_count, width)
    return lax.all_to_all(result, ("patch", "tm"), split_axis=0, concat_axis=1, tiled=True)


def solution(mesh):
    in_specs = (P(("subject", "patch", "tm"), None, None), P(), P(), P(), P())
    out_specs = P(("subject", "patch", "tm"), None, None)
    return jax.shard_map(body, mesh=mesh, in_specs=in_specs, out_specs=out_specs, check_vma=False)
```

```python
import jax
import jax.numpy as jnp
from jax import lax
from jax.experimental import pallas as pl
from jax.experimental.pallas import tpu as pltpu
from jax.sharding import PartitionSpec as P

HEADS = 8

epsilon = 1e-05
floor_score = -1e30


def _layer_norm(rows):
    width = rows.shape[-1]
    centre = jnp.sum(rows, axis=-1, keepdims=True) * (1.0 / width)
    centered = rows - centre
    spread = jnp.sum(centered * centered, axis=-1, keepdims=True) * (1.0 / width)
    return (centered * lax.rsqrt(spread + epsilon)).astype(jnp.bfloat16)


def _attention_block(x_ref, w_copies, wqkv_ref, wout_ref, o_ref, packed_ref, attn_ref, mask_fn):
    rows = x_ref[...].astype(jnp.float32)
    width = rows.shape[-1]
    head_dim = width // HEADS
    normed = _layer_norm(rows)
    for part in range(3):
        if w_copies is not None:
            w_copies[part].wait()
        cols = slice(part * width, (part + 1) * width)
        packed_ref[:, cols] = jnp.dot(
            normed, wqkv_ref[:, cols], preferred_element_type=jnp.float32
        ).astype(jnp.bfloat16)
    factor = head_dim ** (-0.5)
    n_rows = rows.shape[0]
    allowed = mask_fn(n_rows)
    lane = lax.broadcasted_iota(jnp.int32, (1, 2 * head_dim), 1)
    low = lane < head_dim
    for pair in range(HEADS // 2):
        cols = slice(pair * 2 * head_dim, (pair + 1) * 2 * head_dim)
        q2 = packed_ref[:, cols]
        k2 = packed_ref[:, width + cols.start : width + cols.stop]
        v2 = packed_ref[:, 2 * width + cols.start : 2 * width + cols.stop]
        halves = []
        for sel in (low, jnp.logical_not(low)):
            qh = jnp.where(sel, q2, jnp.zeros_like(q2))
            scores = (
                lax.dot_general(
                    qh, k2, (((1,), (1,)), ((), ())), preferred_element_type=jnp.float32
                )
                * factor
            )
            if allowed is not None:
                scores = jnp.where(allowed, scores, floor_score)
            highest = jnp.max(scores, axis=-1, keepdims=True)
            exp_terms = jnp.exp(scores - highest)
            if allowed is not None:
                exp_terms = jnp.where(allowed, exp_terms, 0.0)
            total = jnp.sum(exp_terms, axis=-1, keepdims=True)
            mixture = jnp.dot(
                exp_terms.astype(jnp.bfloat16), v2, preferred_element_type=jnp.float32
            )
            halves.append(mixture / total)
        attn_ref[:, cols] = jnp.where(low, halves[0], halves[1]).astype(jnp.bfloat16)
    if w_copies is not None:
        w_copies[3].wait()
    update = jnp.dot(attn_ref[...], wout_ref[...], preferred_element_type=jnp.float32)
    o_ref[...] = (rows + update).astype(jnp.bfloat16)


def _no_mask(n_rows):
    return None


def _make_causal_mask(group):
    def mask_fn(n_rows):
        r_a = lax.broadcasted_iota(jnp.int32, (n_rows, n_rows), 0)
        r_b = lax.broadcasted_iota(jnp.int32, (n_rows, n_rows), 1)
        return (r_b <= r_a) & (jnp.bitwise_and(r_a - r_b, group - 1) == 0)

    return mask_fn


def _layer_call(rows, qkv_weight, out_weight, mask_fn, rows_in_hbm):
    n_rows, width = rows.shape

    def kernel(x_in, wqkv_hbm, wout_hbm, o_ref, x_vmem, wqkv_ref, wout_ref, packed_ref, attn_ref, sems):
        if rows_in_hbm:
            x_copy = pltpu.make_async_copy(x_in, x_vmem, sems.at[4])
            x_copy.start()
        if rows_in_hbm:
            w_copies = [
                pltpu.make_async_copy(
                    wqkv_hbm.at[:, pl.ds(part * width, width)],
                    wqkv_ref.at[:, pl.ds(part * width, width)],
                    sems.at[part],
                )
                for part in range(3)
            ]
            w_copies.append(pltpu.make_async_copy(wout_hbm, wout_ref, sems.at[3]))
            for copy in w_copies:
                copy.start()
            x_copy.wait()
            _attention_block(
                x_vmem, w_copies, wqkv_ref, wout_ref, o_ref, packed_ref, attn_ref, mask_fn
            )
        else:
            _attention_block(
                x_in, None, wqkv_hbm, wout_hbm, o_ref, packed_ref, attn_ref, mask_fn
            )

    vmem = pl.BlockSpec(memory_space=pltpu.VMEM)
    hbm = pl.BlockSpec(memory_space=pltpu.HBM)
    return pl.pallas_call(
        kernel,
        out_shape=jax.ShapeDtypeStruct((n_rows, width), jnp.bfloat16),
        in_specs=[hbm, hbm, hbm] if rows_in_hbm else [vmem, vmem, vmem],
        out_specs=vmem,
        scratch_shapes=[
            pltpu.VMEM((n_rows, width), jnp.bfloat16),
            pltpu.VMEM((width, 3 * width), jnp.bfloat16),
            pltpu.VMEM((width, width), jnp.bfloat16),
            pltpu.VMEM((n_rows, 3 * width), jnp.bfloat16),
            pltpu.VMEM((n_rows, width), jnp.bfloat16),
            pltpu.SemaphoreType.DMA((5,)),
        ],
        compiler_params=pltpu.CompilerParams(vmem_limit_bytes=48 * 1024 * 1024),
    )(
        pltpu.with_memory_space_constraint(rows, pltpu.HBM) if rows_in_hbm else rows,
        pltpu.with_memory_space_constraint(qkv_weight, pltpu.HBM) if rows_in_hbm else qkv_weight,
        pltpu.with_memory_space_constraint(out_weight, pltpu.HBM) if rows_in_hbm else out_weight,
    )


def body(frames_in, spatial_qkv, spatial_out, temporal_qkv, temporal_out):
    n_frames, n_patches, width = frames_in.shape
    assert n_frames == 1
    group = lax.axis_size(("patch", "tm"))
    hidden = _layer_call(frames_in[0], spatial_qkv, spatial_out, _no_mask, True)
    columns = lax.all_to_all(
        hidden.reshape(group, n_patches // group, width),
        ("patch", "tm"),
        split_axis=0,
        concat_axis=0,
        tiled=True,
    )
    frame_total, column_count, _ = columns.shape
    assert column_count & (column_count - 1) == 0
    result = _layer_call(
        columns.reshape(frame_total * column_count, width),
        temporal_qkv,
        temporal_out,
        _make_causal_mask(column_count),
        False,
    ).reshape(frame_total, column_count, width)
    return lax.all_to_all(result, ("patch", "tm"), split_axis=0, concat_axis=1, tiled=True)


def solution(mesh):
    in_specs = (P(("subject", "patch", "tm"), None, None), P(), P(), P(), P())
    out_specs = P(("subject", "patch", "tm"), None, None)
    return jax.shard_map(body, mesh=mesh, in_specs=in_specs, out_specs=out_specs, check_vma=False)
```

```python
import jax
import jax.numpy as jnp
from jax import lax
from jax.experimental import pallas as pl
from jax.experimental.pallas import tpu as pltpu
from jax.sharding import PartitionSpec as P

HEADS = 8

epsilon = 1e-05
floor_score = -1e30


def _layer_norm(rows):
    width = rows.shape[-1]
    centre = jnp.sum(rows, axis=-1, keepdims=True) * (1.0 / width)
    centered = rows - centre
    spread = jnp.sum(centered * centered, axis=-1, keepdims=True) * (1.0 / width)
    return (centered * lax.rsqrt(spread + epsilon)).astype(jnp.bfloat16)


def _attention_block(x_ref, w_copies, wqkv_ref, wout_ref, o_ref, packed_ref, attn_ref, mask_fn):
    rows = x_ref[...].astype(jnp.float32)
    width = rows.shape[-1]
    head_dim = width // HEADS
    normed = _layer_norm(rows)
    for part in range(3):
        if w_copies is not None:
            w_copies[part].wait()
        cols = slice(part * width, (part + 1) * width)
        packed_ref[:, cols] = jnp.dot(
            normed, wqkv_ref[:, cols], preferred_element_type=jnp.float32
        ).astype(jnp.bfloat16)
    factor = head_dim ** (-0.5)
    n_rows = rows.shape[0]
    lane = lax.broadcasted_iota(jnp.int32, (1, 2 * head_dim), 1)
    low = lane < head_dim
    if mask_fn is None:
        blocks = [(0, n_rows, n_rows)]
    else:
        step = min(128, n_rows)
        blocks = [(r0, step, r0 + step) for r0 in range(0, n_rows, step)]
    for pair in range(HEADS // 2):
        cols = slice(pair * 2 * head_dim, (pair + 1) * 2 * head_dim)
        for r0, n_q, n_k in blocks:
            q2 = packed_ref[r0 : r0 + n_q, cols]
            k2 = packed_ref[:n_k, width + cols.start : width + cols.stop]
            v2 = packed_ref[:n_k, 2 * width + cols.start : 2 * width + cols.stop]
            allowed = None if mask_fn is None else mask_fn(r0, n_q, n_k)
            halves = []
            for sel in (low, jnp.logical_not(low)):
                qh = jnp.where(sel, q2, jnp.zeros_like(q2))
                scores = (
                    lax.dot_general(
                        qh, k2, (((1,), (1,)), ((), ())), preferred_element_type=jnp.float32
                    )
                    * factor
                )
                if allowed is not None:
                    scores = jnp.where(allowed, scores, floor_score)
                highest = jnp.max(scores, axis=-1, keepdims=True)
                exp_terms = jnp.exp(scores - highest)
                if allowed is not None:
                    exp_terms = jnp.where(allowed, exp_terms, 0.0)
                total = jnp.sum(exp_terms, axis=-1, keepdims=True)
                mixture = jnp.dot(
                    exp_terms.astype(jnp.bfloat16), v2, preferred_element_type=jnp.float32
                )
                halves.append(mixture * (1.0 / total))
            attn_ref[r0 : r0 + n_q, cols] = jnp.where(low, halves[0], halves[1]).astype(
                jnp.bfloat16
            )
    if w_copies is not None:
        w_copies[3].wait()
    update = jnp.dot(attn_ref[...], wout_ref[...], preferred_element_type=jnp.float32)
    o_ref[...] = (rows + update).astype(jnp.bfloat16)


def _make_causal_mask(group):
    def mask_fn(r0, n_q, n_k):
        r_a = lax.broadcasted_iota(jnp.int32, (n_q, n_k), 0) + r0
        r_b = lax.broadcasted_iota(jnp.int32, (n_q, n_k), 1)
        return (r_b <= r_a) & (jnp.bitwise_and(r_a - r_b, group - 1) == 0)

    return mask_fn


def _layer_call(rows, qkv_weight, out_weight, mask_fn, rows_in_hbm):
    n_rows, width = rows.shape

    def kernel(x_in, wqkv_hbm, wout_hbm, o_ref, x_vmem, wqkv_ref, wout_ref, packed_ref, attn_ref, sems):
        if rows_in_hbm:
            x_copy = pltpu.make_async_copy(x_in, x_vmem, sems.at[4])
            x_copy.start()
        if rows_in_hbm:
            w_copies = [
                pltpu.make_async_copy(
                    wqkv_hbm.at[:, pl.ds(part * width, width)],
                    wqkv_ref.at[:, pl.ds(part * width, width)],
                    sems.at[part],
                )
                for part in range(3)
            ]
            w_copies.append(pltpu.make_async_copy(wout_hbm, wout_ref, sems.at[3]))
            for copy in w_copies:
                copy.start()
            x_copy.wait()
            _attention_block(
                x_vmem, w_copies, wqkv_ref, wout_ref, o_ref, packed_ref, attn_ref, mask_fn
            )
        else:
            _attention_block(
                x_in, None, wqkv_hbm, wout_hbm, o_ref, packed_ref, attn_ref, mask_fn
            )

    vmem = pl.BlockSpec(memory_space=pltpu.VMEM)
    hbm = pl.BlockSpec(memory_space=pltpu.HBM)
    return pl.pallas_call(
        kernel,
        out_shape=jax.ShapeDtypeStruct((n_rows, width), jnp.bfloat16),
        in_specs=[hbm, hbm, hbm] if rows_in_hbm else [vmem, vmem, vmem],
        out_specs=vmem,
        scratch_shapes=[
            pltpu.VMEM((n_rows, width), jnp.bfloat16),
            pltpu.VMEM((width, 3 * width), jnp.bfloat16),
            pltpu.VMEM((width, width), jnp.bfloat16),
            pltpu.VMEM((n_rows, 3 * width), jnp.bfloat16),
            pltpu.VMEM((n_rows, width), jnp.bfloat16),
            pltpu.SemaphoreType.DMA((5,)),
        ],
        compiler_params=pltpu.CompilerParams(vmem_limit_bytes=48 * 1024 * 1024),
    )(
        pltpu.with_memory_space_constraint(rows, pltpu.HBM) if rows_in_hbm else rows,
        pltpu.with_memory_space_constraint(qkv_weight, pltpu.HBM) if rows_in_hbm else qkv_weight,
        pltpu.with_memory_space_constraint(out_weight, pltpu.HBM) if rows_in_hbm else out_weight,
    )


def body(frames_in, spatial_qkv, spatial_out, temporal_qkv, temporal_out):
    n_frames, n_patches, width = frames_in.shape
    assert n_frames == 1
    group = lax.axis_size(("patch", "tm"))
    hidden = _layer_call(frames_in[0], spatial_qkv, spatial_out, None, True)
    columns = lax.all_to_all(
        hidden.reshape(group, n_patches // group, width),
        ("patch", "tm"),
        split_axis=0,
        concat_axis=0,
        tiled=True,
    )
    frame_total, column_count, _ = columns.shape
    assert column_count & (column_count - 1) == 0
    result = _layer_call(
        columns.reshape(frame_total * column_count, width),
        temporal_qkv,
        temporal_out,
        _make_causal_mask(column_count),
        False,
    ).reshape(frame_total, column_count, width)
    return lax.all_to_all(result, ("patch", "tm"), split_axis=0, concat_axis=1, tiled=True)


def solution(mesh):
    in_specs = (P(("subject", "patch", "tm"), None, None), P(), P(), P(), P())
    out_specs = P(("subject", "patch", "tm"), None, None)
    return jax.shard_map(body, mesh=mesh, in_specs=in_specs, out_specs=out_specs, check_vma=False)
```

```python
import jax
import jax.numpy as jnp
from jax import lax
from jax.experimental import pallas as pl
from jax.experimental.pallas import tpu as pltpu
from jax.sharding import PartitionSpec as P

HEADS = 8
_GROUPS = 2

epsilon = 1e-05
floor_score = -1e30


def _layer_norm(rows):
    width = rows.shape[-1]
    centre = jnp.sum(rows, axis=-1, keepdims=True) * (1.0 / width)
    centered = rows - centre
    spread = jnp.sum(centered * centered, axis=-1, keepdims=True) * (1.0 / width)
    return (centered * lax.rsqrt(spread + epsilon)).astype(jnp.bfloat16)


def _attention_block(x_ref, w_copies, wqkv_ref, wout_ref, o_ref, packed_ref, attn_ref, mask_fn):
    rows = x_ref[...].astype(jnp.float32)
    width = rows.shape[-1]
    head_dim = width // HEADS
    normed = _layer_norm(rows)
    factor = head_dim ** (-0.5)
    n_rows = rows.shape[0]
    allowed = mask_fn(n_rows)
    lane = lax.broadcasted_iota(jnp.int32, (1, 2 * head_dim), 1)
    low = lane < head_dim
    group_width = width // _GROUPS
    for pair in range(HEADS // 2):
        group = pair * 2 * head_dim // group_width
        if pair * 2 * head_dim % group_width == 0:
            for part in range(3):
                if w_copies is not None:
                    w_copies[group * 3 + part].wait()
                cols = slice(part * width + group * group_width, part * width + (group + 1) * group_width)
                packed_ref[:, cols] = jnp.dot(
                    normed, wqkv_ref[:, cols], preferred_element_type=jnp.float32
                ).astype(jnp.bfloat16)
        cols = slice(pair * 2 * head_dim, (pair + 1) * 2 * head_dim)
        q2 = packed_ref[:, cols]
        k2 = packed_ref[:, width + cols.start : width + cols.stop]
        v2 = packed_ref[:, 2 * width + cols.start : 2 * width + cols.stop]
        halves = []
        for sel in (low, jnp.logical_not(low)):
            qh = jnp.where(sel, q2, jnp.zeros_like(q2))
            scores = (
                lax.dot_general(
                    qh, k2, (((1,), (1,)), ((), ())), preferred_element_type=jnp.float32
                )
                * factor
            )
            if allowed is not None:
                scores = jnp.where(allowed, scores, floor_score)
            highest = jnp.max(scores, axis=-1, keepdims=True)
            exp_terms = jnp.exp(scores - highest)
            if allowed is not None:
                exp_terms = jnp.where(allowed, exp_terms, 0.0)
            total = jnp.sum(exp_terms, axis=-1, keepdims=True)
            mixture = jnp.dot(
                exp_terms.astype(jnp.bfloat16), v2, preferred_element_type=jnp.float32
            )
            halves.append(mixture / total)
        attn_ref[:, cols] = jnp.where(low, halves[0], halves[1]).astype(jnp.bfloat16)
    if w_copies is not None:
        w_copies[-1].wait()
    update = jnp.dot(attn_ref[...], wout_ref[...], preferred_element_type=jnp.float32)
    o_ref[...] = (rows + update).astype(jnp.bfloat16)


def _no_mask(n_rows):
    return None


def _make_causal_mask(group):
    def mask_fn(n_rows):
        r_a = lax.broadcasted_iota(jnp.int32, (n_rows, n_rows), 0)
        r_b = lax.broadcasted_iota(jnp.int32, (n_rows, n_rows), 1)
        return (r_b <= r_a) & (jnp.bitwise_and(r_a - r_b, group - 1) == 0)

    return mask_fn


def _layer_call(rows, qkv_weight, out_weight, mask_fn, rows_in_hbm):
    n_rows, width = rows.shape

    def kernel(x_in, wqkv_hbm, wout_hbm, o_ref, x_vmem, wqkv_ref, wout_ref, packed_ref, attn_ref, sems):
        if rows_in_hbm:
            x_copy = pltpu.make_async_copy(x_in, x_vmem, sems.at[3 * _GROUPS + 1])
            x_copy.start()
        if rows_in_hbm:
            group_width = width // _GROUPS
            w_copies = [
                pltpu.make_async_copy(
                    wqkv_hbm.at[:, pl.ds(part * width + group * group_width, group_width)],
                    wqkv_ref.at[:, pl.ds(part * width + group * group_width, group_width)],
                    sems.at[group * 3 + part],
                )
                for group in range(_GROUPS)
                for part in range(3)
            ]
            w_copies.append(pltpu.make_async_copy(wout_hbm, wout_ref, sems.at[3 * _GROUPS]))
            for copy in w_copies:
                copy.start()
            x_copy.wait()
            _attention_block(
                x_vmem, w_copies, wqkv_ref, wout_ref, o_ref, packed_ref, attn_ref, mask_fn
            )
        else:
            _attention_block(
                x_in, None, wqkv_hbm, wout_hbm, o_ref, packed_ref, attn_ref, mask_fn
            )

    vmem = pl.BlockSpec(memory_space=pltpu.VMEM)
    hbm = pl.BlockSpec(memory_space=pltpu.HBM)
    return pl.pallas_call(
        kernel,
        out_shape=jax.ShapeDtypeStruct((n_rows, width), jnp.bfloat16),
        in_specs=[hbm, hbm, hbm] if rows_in_hbm else [vmem, vmem, vmem],
        out_specs=vmem,
        scratch_shapes=[
            pltpu.VMEM((n_rows, width), jnp.bfloat16),
            pltpu.VMEM((width, 3 * width), jnp.bfloat16),
            pltpu.VMEM((width, width), jnp.bfloat16),
            pltpu.VMEM((n_rows, 3 * width), jnp.bfloat16),
            pltpu.VMEM((n_rows, width), jnp.bfloat16),
            pltpu.SemaphoreType.DMA((3 * _GROUPS + 2,)),
        ],
        compiler_params=pltpu.CompilerParams(vmem_limit_bytes=48 * 1024 * 1024),
    )(
        pltpu.with_memory_space_constraint(rows, pltpu.HBM) if rows_in_hbm else rows,
        pltpu.with_memory_space_constraint(qkv_weight, pltpu.HBM) if rows_in_hbm else qkv_weight,
        pltpu.with_memory_space_constraint(out_weight, pltpu.HBM) if rows_in_hbm else out_weight,
    )


def body(frames_in, spatial_qkv, spatial_out, temporal_qkv, temporal_out):
    n_frames, n_patches, width = frames_in.shape
    assert n_frames == 1
    group = lax.axis_size(("patch", "tm"))
    hidden = _layer_call(frames_in[0], spatial_qkv, spatial_out, _no_mask, True)
    columns = lax.all_to_all(
        hidden.reshape(group, n_patches // group, width),
        ("patch", "tm"),
        split_axis=0,
        concat_axis=0,
        tiled=True,
    )
    frame_total, column_count, _ = columns.shape
    assert column_count & (column_count - 1) == 0
    result = _layer_call(
        columns.reshape(frame_total * column_count, width),
        temporal_qkv,
        temporal_out,
        _make_causal_mask(column_count),
        False,
    ).reshape(frame_total, column_count, width)
    return lax.all_to_all(result, ("patch", "tm"), split_axis=0, concat_axis=1, tiled=True)


def solution(mesh):
    in_specs = (P(("subject", "patch", "tm"), None, None), P(), P(), P(), P())
    out_specs = P(("subject", "patch", "tm"), None, None)
    return jax.shard_map(body, mesh=mesh, in_specs=in_specs, out_specs=out_specs, check_vma=False)
```

```python
import jax
import jax.numpy as jnp
from jax import lax
from jax.experimental import pallas as pl
from jax.experimental.pallas import tpu as pltpu
from jax.sharding import PartitionSpec as P

HEADS = 8

epsilon = 1e-05
floor_score = -1e30


def _layer_norm(rows):
    width = rows.shape[-1]
    centre = jnp.sum(rows, axis=-1, keepdims=True) * (1.0 / width)
    centered = rows - centre
    spread = jnp.sum(centered * centered, axis=-1, keepdims=True) * (1.0 / width)
    return (centered * lax.rsqrt(spread + epsilon)).astype(jnp.bfloat16)


def _attention_block(x_ref, w_copies, wqkv_ref, wout_ref, o_ref, packed_ref, attn_ref, mask_fn):
    rows = x_ref[...].astype(jnp.float32)
    width = rows.shape[-1]
    head_dim = width // HEADS
    normed = _layer_norm(rows)
    for part in range(3):
        if w_copies is not None:
            w_copies[part].wait()
        cols = slice(part * width, (part + 1) * width)
        packed_ref[:, cols] = jnp.dot(
            normed, wqkv_ref[:, cols], preferred_element_type=jnp.float32
        ).astype(jnp.bfloat16)
    factor = head_dim ** (-0.5)
    n_rows = rows.shape[0]
    allowed = mask_fn(n_rows)
    lane = lax.broadcasted_iota(jnp.int32, (1, 2 * head_dim), 1)
    low = lane < head_dim
    for pair in range(HEADS // 2):
        cols = slice(pair * 2 * head_dim, (pair + 1) * 2 * head_dim)
        q2 = packed_ref[:, cols]
        k2 = packed_ref[:, width + cols.start : width + cols.stop]
        v2 = packed_ref[:, 2 * width + cols.start : 2 * width + cols.stop]
        halves = []
        for sel in (low, jnp.logical_not(low)):
            qh = jnp.where(sel, q2, jnp.zeros_like(q2))
            scores = (
                lax.dot_general(
                    qh, k2, (((1,), (1,)), ((), ())), preferred_element_type=jnp.float32
                )
                * factor
            )
            if allowed is not None:
                scores = jnp.where(allowed, scores, floor_score)
            highest = jnp.max(scores, axis=-1, keepdims=True)
            exp_terms = jnp.exp(scores - highest)
            if allowed is not None:
                exp_terms = jnp.where(allowed, exp_terms, 0.0)
            total = jnp.sum(exp_terms, axis=-1, keepdims=True)
            mixture = jnp.dot(
                exp_terms.astype(jnp.bfloat16), v2, preferred_element_type=jnp.float32
            )
            halves.append(mixture / total)
        attn_ref[:, cols] = jnp.where(low, halves[0], halves[1]).astype(jnp.bfloat16)
    if wout_ref is None:
        o_ref[...] = attn_ref[...]
        return
    if w_copies is not None:
        w_copies[3].wait()
    update = jnp.dot(attn_ref[...], wout_ref[...], preferred_element_type=jnp.float32)
    o_ref[...] = (rows + update).astype(jnp.bfloat16)


def _no_mask(n_rows):
    return None


def _make_causal_mask(group):
    def mask_fn(n_rows):
        r_a = lax.broadcasted_iota(jnp.int32, (n_rows, n_rows), 0)
        r_b = lax.broadcasted_iota(jnp.int32, (n_rows, n_rows), 1)
        return (r_b <= r_a) & (jnp.bitwise_and(r_a - r_b, group - 1) == 0)

    return mask_fn


def _layer_call(rows, qkv_weight, out_weight, mask_fn, rows_in_hbm):
    n_rows, width = rows.shape

    def kernel(x_in, wqkv_hbm, wout_hbm, o_ref, x_vmem, wqkv_ref, wout_ref, packed_ref, attn_ref, sems):
        if rows_in_hbm:
            x_copy = pltpu.make_async_copy(x_in, x_vmem, sems.at[4])
            x_copy.start()
        if rows_in_hbm:
            w_copies = [
                pltpu.make_async_copy(
                    wqkv_hbm.at[:, pl.ds(part * width, width)],
                    wqkv_ref.at[:, pl.ds(part * width, width)],
                    sems.at[part],
                )
                for part in range(3)
            ]
            w_copies.append(pltpu.make_async_copy(wout_hbm, wout_ref, sems.at[3]))
            for copy in w_copies:
                copy.start()
            x_copy.wait()
            _attention_block(
                x_vmem, w_copies, wqkv_ref, wout_ref, o_ref, packed_ref, attn_ref, mask_fn
            )
        else:
            _attention_block(
                x_in, None, wqkv_hbm, None, o_ref, packed_ref, attn_ref, mask_fn
            )

    vmem = pl.BlockSpec(memory_space=pltpu.VMEM)
    hbm = pl.BlockSpec(memory_space=pltpu.HBM)
    return pl.pallas_call(
        kernel,
        out_shape=jax.ShapeDtypeStruct((n_rows, width), jnp.bfloat16),
        in_specs=[hbm, hbm, hbm] if rows_in_hbm else [vmem, vmem, vmem],
        out_specs=vmem,
        scratch_shapes=[
            pltpu.VMEM((n_rows, width), jnp.bfloat16),
            pltpu.VMEM((width, 3 * width), jnp.bfloat16),
            pltpu.VMEM((width, width), jnp.bfloat16),
            pltpu.VMEM((n_rows, 3 * width), jnp.bfloat16),
            pltpu.VMEM((n_rows, width), jnp.bfloat16),
            pltpu.SemaphoreType.DMA((5,)),
        ],
        compiler_params=pltpu.CompilerParams(vmem_limit_bytes=48 * 1024 * 1024),
    )(
        pltpu.with_memory_space_constraint(rows, pltpu.HBM) if rows_in_hbm else rows,
        pltpu.with_memory_space_constraint(qkv_weight, pltpu.HBM) if rows_in_hbm else qkv_weight,
        pltpu.with_memory_space_constraint(out_weight, pltpu.HBM) if rows_in_hbm else out_weight,
    )


def _project_call(hidden, attn, out_weight):
    n_rows, width = hidden.shape

    def kernel(h_ref, a_ref, w_ref, o_ref):
        update = jnp.dot(a_ref[...], w_ref[...], preferred_element_type=jnp.float32)
        o_ref[...] = (h_ref[...].astype(jnp.float32) + update).astype(jnp.bfloat16)

    vmem = pl.BlockSpec(memory_space=pltpu.VMEM)
    return pl.pallas_call(
        kernel,
        out_shape=jax.ShapeDtypeStruct((n_rows, width), jnp.bfloat16),
        in_specs=[vmem, vmem, vmem],
        out_specs=vmem,
    )(hidden, attn, out_weight)


def body(frames_in, spatial_qkv, spatial_out, temporal_qkv, temporal_out):
    n_frames, n_patches, width = frames_in.shape
    assert n_frames == 1
    group = lax.axis_size(("patch", "tm"))
    hidden = _layer_call(frames_in[0], spatial_qkv, spatial_out, _no_mask, True)
    columns = lax.all_to_all(
        hidden.reshape(group, n_patches // group, width),
        ("patch", "tm"),
        split_axis=0,
        concat_axis=0,
        tiled=True,
    )
    frame_total, column_count, _ = columns.shape
    assert column_count & (column_count - 1) == 0
    result = _layer_call(
        columns.reshape(frame_total * column_count, width),
        temporal_qkv,
        temporal_out,
        _make_causal_mask(column_count),
        False,
    ).reshape(frame_total, column_count, width)
    attn = lax.all_to_all(result, ("patch", "tm"), split_axis=0, concat_axis=1, tiled=True)
    return _project_call(hidden, attn.reshape(n_patches, width), temporal_out)[None]


def solution(mesh):
    in_specs = (P(("subject", "patch", "tm"), None, None), P(), P(), P(), P())
    out_specs = P(("subject", "patch", "tm"), None, None)
    return jax.shard_map(body, mesh=mesh, in_specs=in_specs, out_specs=out_specs, check_vma=False)
```

```python
import jax
import jax.numpy as jnp
from jax import lax
from jax.experimental import pallas as pl
from jax.experimental.pallas import tpu as pltpu
from jax.sharding import PartitionSpec as P

HEADS = 8

epsilon = 1e-05
floor_score = -1e30


def _layer_norm(rows):
    width = rows.shape[-1]
    centre = jnp.sum(rows, axis=-1, keepdims=True) * (1.0 / width)
    centered = rows - centre
    spread = jnp.sum(centered * centered, axis=-1, keepdims=True) * (1.0 / width)
    return (centered * lax.rsqrt(spread + epsilon)).astype(jnp.bfloat16)


def _attention_block(x_ref, w_copies, wqkv_ref, wout_ref, o_ref, packed_ref, attn_ref, mask_fn):
    rows = x_ref[...].astype(jnp.float32)
    width = rows.shape[-1]
    head_dim = width // HEADS
    normed = _layer_norm(rows)
    if w_copies is not None:
        for part in range(3):
            w_copies[part].wait()
    packed_ref[...] = jnp.dot(
        normed, wqkv_ref[...], preferred_element_type=jnp.float32
    ).astype(jnp.bfloat16)
    factor = head_dim ** (-0.5)
    n_rows = rows.shape[0]
    allowed = mask_fn(n_rows)
    lane = lax.broadcasted_iota(jnp.int32, (1, 2 * head_dim), 1)
    low = lane < head_dim
    for pair in range(HEADS // 2):
        cols = slice(pair * 2 * head_dim, (pair + 1) * 2 * head_dim)
        q2 = packed_ref[:, cols]
        k2 = packed_ref[:, width + cols.start : width + cols.stop]
        v2 = packed_ref[:, 2 * width + cols.start : 2 * width + cols.stop]
        halves = []
        for sel in (low, jnp.logical_not(low)):
            qh = jnp.where(sel, q2, jnp.zeros_like(q2))
            scores = (
                lax.dot_general(
                    qh, k2, (((1,), (1,)), ((), ())), preferred_element_type=jnp.float32
                )
                * factor
            )
            if allowed is not None:
                scores = jnp.where(allowed, scores, floor_score)
            highest = jnp.max(scores, axis=-1, keepdims=True)
            exp_terms = jnp.exp(scores - highest)
            if allowed is not None:
                exp_terms = jnp.where(allowed, exp_terms, 0.0)
            total = jnp.sum(exp_terms, axis=-1, keepdims=True)
            mixture = jnp.dot(
                exp_terms.astype(jnp.bfloat16), v2, preferred_element_type=jnp.float32
            )
            halves.append(mixture / total)
        attn_ref[:, cols] = jnp.where(low, halves[0], halves[1]).astype(jnp.bfloat16)
    if w_copies is not None:
        w_copies[3].wait()
    update = jnp.dot(attn_ref[...], wout_ref[...], preferred_element_type=jnp.float32)
    o_ref[...] = (rows + update).astype(jnp.bfloat16)


def _no_mask(n_rows):
    return None


def _make_causal_mask(group):
    def mask_fn(n_rows):
        r_a = lax.broadcasted_iota(jnp.int32, (n_rows, n_rows), 0)
        r_b = lax.broadcasted_iota(jnp.int32, (n_rows, n_rows), 1)
        return (r_b <= r_a) & (jnp.bitwise_and(r_a - r_b, group - 1) == 0)

    return mask_fn


def _layer_call(rows, qkv_weight, out_weight, mask_fn, rows_in_hbm):
    n_rows, width = rows.shape

    def kernel(x_in, wqkv_hbm, wout_hbm, o_ref, x_vmem, wqkv_ref, wout_ref, packed_ref, attn_ref, sems):
        if rows_in_hbm:
            x_copy = pltpu.make_async_copy(x_in, x_vmem, sems.at[4])
            x_copy.start()
        if rows_in_hbm:
            w_copies = [
                pltpu.make_async_copy(
                    wqkv_hbm.at[:, pl.ds(part * width, width)],
                    wqkv_ref.at[:, pl.ds(part * width, width)],
                    sems.at[part],
                )
                for part in range(3)
            ]
            w_copies.append(pltpu.make_async_copy(wout_hbm, wout_ref, sems.at[3]))
            for copy in w_copies:
                copy.start()
            x_copy.wait()
            _attention_block(
                x_vmem, w_copies, wqkv_ref, wout_ref, o_ref, packed_ref, attn_ref, mask_fn
            )
        else:
            _attention_block(
                x_in, None, wqkv_hbm, wout_hbm, o_ref, packed_ref, attn_ref, mask_fn
            )

    vmem = pl.BlockSpec(memory_space=pltpu.VMEM)
    hbm = pl.BlockSpec(memory_space=pltpu.HBM)
    return pl.pallas_call(
        kernel,
        out_shape=jax.ShapeDtypeStruct((n_rows, width), jnp.bfloat16),
        in_specs=[hbm, hbm, hbm] if rows_in_hbm else [vmem, vmem, vmem],
        out_specs=vmem,
        scratch_shapes=[
            pltpu.VMEM((n_rows, width), jnp.bfloat16),
            pltpu.VMEM((width, 3 * width), jnp.bfloat16),
            pltpu.VMEM((width, width), jnp.bfloat16),
            pltpu.VMEM((n_rows, 3 * width), jnp.bfloat16),
            pltpu.VMEM((n_rows, width), jnp.bfloat16),
            pltpu.SemaphoreType.DMA((5,)),
        ],
        compiler_params=pltpu.CompilerParams(vmem_limit_bytes=48 * 1024 * 1024),
    )(
        pltpu.with_memory_space_constraint(rows, pltpu.HBM) if rows_in_hbm else rows,
        pltpu.with_memory_space_constraint(qkv_weight, pltpu.HBM) if rows_in_hbm else qkv_weight,
        pltpu.with_memory_space_constraint(out_weight, pltpu.HBM) if rows_in_hbm else out_weight,
    )


def body(frames_in, spatial_qkv, spatial_out, temporal_qkv, temporal_out):
    n_frames, n_patches, width = frames_in.shape
    assert n_frames == 1
    group = lax.axis_size(("patch", "tm"))
    hidden = _layer_call(frames_in[0], spatial_qkv, spatial_out, _no_mask, True)
    columns = lax.all_to_all(
        hidden.reshape(group, n_patches // group, width),
        ("patch", "tm"),
        split_axis=0,
        concat_axis=0,
        tiled=True,
    )
    frame_total, column_count, _ = columns.shape
    assert column_count & (column_count - 1) == 0
    result = _layer_call(
        columns.reshape(frame_total * column_count, width),
        temporal_qkv,
        temporal_out,
        _make_causal_mask(column_count),
        False,
    ).reshape(frame_total, column_count, width)
    return lax.all_to_all(result, ("patch", "tm"), split_axis=0, concat_axis=1, tiled=True)


def solution(mesh):
    in_specs = (P(("subject", "patch", "tm"), None, None), P(), P(), P(), P())
    out_specs = P(("subject", "patch", "tm"), None, None)
    return jax.shard_map(body, mesh=mesh, in_specs=in_specs, out_specs=out_specs, check_vma=False)
```

```python
import jax
import jax.numpy as jnp
from jax import lax
from jax.experimental import pallas as pl
from jax.experimental.pallas import tpu as pltpu
from jax.sharding import PartitionSpec as P

HEADS = 8

epsilon = 1e-05
floor_score = -1e30


def _layer_norm(rows):
    width = rows.shape[-1]
    centre = jnp.sum(rows, axis=-1, keepdims=True) * (1.0 / width)
    centered = rows - centre
    spread = jnp.sum(centered * centered, axis=-1, keepdims=True) * (1.0 / width)
    return (centered * lax.rsqrt(spread + epsilon)).astype(jnp.bfloat16)


def _attention_block(
    x_ref, w_copies, wqkv_ref, wout_ref, o_ref, packed_ref, attn_ref, mask_fn, after_qkv=None
):
    rows = x_ref[...].astype(jnp.float32)
    width = rows.shape[-1]
    head_dim = width // HEADS
    normed = _layer_norm(rows)
    if w_copies is not None:
        for part in range(3):
            w_copies[part].wait()
    if after_qkv is not None:
        after_qkv.start()
    packed_ref[...] = jnp.dot(
        normed, wqkv_ref[...], preferred_element_type=jnp.float32
    ).astype(jnp.bfloat16)
    factor = head_dim ** (-0.5)
    n_rows = rows.shape[0]
    allowed = mask_fn(n_rows)
    lane = lax.broadcasted_iota(jnp.int32, (1, 2 * head_dim), 1)
    low = lane < head_dim
    for pair in range(HEADS // 2):
        cols = slice(pair * 2 * head_dim, (pair + 1) * 2 * head_dim)
        q2 = packed_ref[:, cols]
        k2 = packed_ref[:, width + cols.start : width + cols.stop]
        v2 = packed_ref[:, 2 * width + cols.start : 2 * width + cols.stop]
        halves = []
        for sel in (low, jnp.logical_not(low)):
            qh = jnp.where(sel, q2, jnp.zeros_like(q2))
            scores = (
                lax.dot_general(
                    qh, k2, (((1,), (1,)), ((), ())), preferred_element_type=jnp.float32
                )
                * factor
            )
            if allowed is not None:
                scores = jnp.where(allowed, scores, floor_score)
            highest = jnp.max(scores, axis=-1, keepdims=True)
            exp_terms = jnp.exp(scores - highest)
            if allowed is not None:
                exp_terms = jnp.where(allowed, exp_terms, 0.0)
            total = jnp.sum(exp_terms, axis=-1, keepdims=True)
            mixture = jnp.dot(
                exp_terms.astype(jnp.bfloat16), v2, preferred_element_type=jnp.float32
            )
            halves.append(mixture / total)
        attn_ref[:, cols] = jnp.where(low, halves[0], halves[1]).astype(jnp.bfloat16)
    if w_copies is not None:
        w_copies[3].wait()
    update = jnp.dot(attn_ref[...], wout_ref[...], preferred_element_type=jnp.float32)
    o_ref[...] = (rows + update).astype(jnp.bfloat16)
    if after_qkv is not None:
        after_qkv.wait()


class _Pair:
    def __init__(self, copies):
        self.copies = copies

    def start(self):
        for c in self.copies:
            c.start()

    def wait(self):
        for c in self.copies:
            c.wait()


def _no_mask(n_rows):
    return None


def _make_causal_mask(group):
    def mask_fn(n_rows):
        r_a = lax.broadcasted_iota(jnp.int32, (n_rows, n_rows), 0)
        r_b = lax.broadcasted_iota(jnp.int32, (n_rows, n_rows), 1)
        return (r_b <= r_a) & (jnp.bitwise_and(r_a - r_b, group - 1) == 0)

    return mask_fn


def _spatial_call(rows, qkv_weight, out_weight, next_qkv, next_out):
    n_rows, width = rows.shape

    def kernel(x_in, wqkv_hbm, wout_hbm, nqkv_hbm, nout_hbm, o_ref, nqkv_ref, nout_ref,
               x_vmem, wqkv_ref, wout_ref, packed_ref, attn_ref, sems):
        x_copy = pltpu.make_async_copy(x_in, x_vmem, sems.at[4])
        x_copy.start()
        w_copies = [
            pltpu.make_async_copy(
                wqkv_hbm.at[:, pl.ds(part * width, width)],
                wqkv_ref.at[:, pl.ds(part * width, width)],
                sems.at[part],
            )
            for part in range(3)
        ]
        w_copies.append(pltpu.make_async_copy(wout_hbm, wout_ref, sems.at[3]))
        for copy in w_copies:
            copy.start()
        after = _Pair([
            pltpu.make_async_copy(nqkv_hbm, nqkv_ref, sems.at[5]),
            pltpu.make_async_copy(nout_hbm, nout_ref, sems.at[6]),
        ])
        x_copy.wait()
        _attention_block(
            x_vmem, w_copies, wqkv_ref, wout_ref, o_ref, packed_ref, attn_ref, _no_mask, after
        )

    vmem = pl.BlockSpec(memory_space=pltpu.VMEM)
    hbm = pl.BlockSpec(memory_space=pltpu.HBM)
    return pl.pallas_call(
        kernel,
        out_shape=(
            jax.ShapeDtypeStruct((n_rows, width), jnp.bfloat16),
            jax.ShapeDtypeStruct(next_qkv.shape, next_qkv.dtype),
            jax.ShapeDtypeStruct(next_out.shape, next_out.dtype),
        ),
        in_specs=[hbm] * 5,
        out_specs=(vmem, vmem, vmem),
        scratch_shapes=[
            pltpu.VMEM((n_rows, width), jnp.bfloat16),
            pltpu.VMEM((width, 3 * width), jnp.bfloat16),
            pltpu.VMEM((width, width), jnp.bfloat16),
            pltpu.VMEM((n_rows, 3 * width), jnp.bfloat16),
            pltpu.VMEM((n_rows, width), jnp.bfloat16),
            pltpu.SemaphoreType.DMA((7,)),
        ],
        compiler_params=pltpu.CompilerParams(vmem_limit_bytes=48 * 1024 * 1024),
    )(*[pltpu.with_memory_space_constraint(a, pltpu.HBM) for a in (rows, qkv_weight, out_weight, next_qkv, next_out)])


def _temporal_call(rows, qkv_weight, out_weight, mask_fn):
    n_rows, width = rows.shape

    def kernel(x_in, wqkv_in, wout_in, o_ref, packed_ref, attn_ref):
        _attention_block(x_in, None, wqkv_in, wout_in, o_ref, packed_ref, attn_ref, mask_fn)

    vmem = pl.BlockSpec(memory_space=pltpu.VMEM)
    return pl.pallas_call(
        kernel,
        out_shape=jax.ShapeDtypeStruct((n_rows, width), jnp.bfloat16),
        in_specs=[vmem, vmem, vmem],
        out_specs=vmem,
        scratch_shapes=[
            pltpu.VMEM((n_rows, 3 * width), jnp.bfloat16),
            pltpu.VMEM((n_rows, width), jnp.bfloat16),
        ],
        compiler_params=pltpu.CompilerParams(vmem_limit_bytes=48 * 1024 * 1024),
    )(rows, qkv_weight, out_weight)


def body(frames_in, spatial_qkv, spatial_out, temporal_qkv, temporal_out):
    n_frames, n_patches, width = frames_in.shape
    assert n_frames == 1
    group = lax.axis_size(("patch", "tm"))
    hidden, t_qkv, t_out = _spatial_call(
        frames_in[0], spatial_qkv, spatial_out, temporal_qkv, temporal_out
    )
    columns = lax.all_to_all(
        hidden.reshape(group, n_patches // group, width),
        ("patch", "tm"),
        split_axis=0,
        concat_axis=0,
        tiled=True,
    )
    frame_total, column_count, _ = columns.shape
    assert column_count & (column_count - 1) == 0
    result = _temporal_call(
        columns.reshape(frame_total * column_count, width),
        t_qkv,
        t_out,
        _make_causal_mask(column_count),
    ).reshape(frame_total, column_count, width)
    return lax.all_to_all(result, ("patch", "tm"), split_axis=0, concat_axis=1, tiled=True)


def solution(mesh):
    in_specs = (P(("subject", "patch", "tm"), None, None), P(), P(), P(), P())
    out_specs = P(("subject", "patch", "tm"), None, None)
    return jax.shard_map(body, mesh=mesh, in_specs=in_specs, out_specs=out_specs, check_vma=False)
```

```python
import jax
import jax.numpy as jnp
from jax import lax
from jax.experimental import pallas as pl
from jax.experimental.pallas import tpu as pltpu
from jax.sharding import PartitionSpec as P

HEADS = 8

epsilon = 1e-05
floor_score = -1e30


def _layer_norm(rows):
    width = rows.shape[-1]
    centre = jnp.sum(rows, axis=-1, keepdims=True) * (1.0 / width)
    centered = rows - centre
    spread = jnp.sum(centered * centered, axis=-1, keepdims=True) * (1.0 / width)
    return (centered * lax.rsqrt(spread + epsilon)).astype(jnp.bfloat16)


def _attention_block(
    x_ref, w_copies, wqkv_ref, wout_ref, o_ref, packed_ref, attn_ref, mask_fn, after_qkv=None
):
    rows = x_ref[...].astype(jnp.float32)
    width = rows.shape[-1]
    head_dim = width // HEADS
    normed = _layer_norm(rows)
    if w_copies is not None:
        for part in range(3):
            w_copies[part].wait()
    if after_qkv is not None:
        after_qkv.start()
    packed_ref[...] = jnp.dot(
        normed, wqkv_ref[...], preferred_element_type=jnp.float32
    ).astype(jnp.bfloat16)
    factor = head_dim ** (-0.5)
    n_rows = rows.shape[0]
    allowed = mask_fn(n_rows)
    lane = lax.broadcasted_iota(jnp.int32, (1, 2 * head_dim), 1)
    low = lane < head_dim
    for pair in range(HEADS // 2):
        cols = slice(pair * 2 * head_dim, (pair + 1) * 2 * head_dim)
        q2 = packed_ref[:, cols]
        k2 = packed_ref[:, width + cols.start : width + cols.stop]
        v2 = packed_ref[:, 2 * width + cols.start : 2 * width + cols.stop]
        halves = []
        for sel in (low, jnp.logical_not(low)):
            qh = jnp.where(sel, q2, jnp.zeros_like(q2))
            scores = (
                lax.dot_general(
                    qh, k2, (((1,), (1,)), ((), ())), preferred_element_type=jnp.float32
                )
                * factor
            )
            if allowed is not None:
                scores = jnp.where(allowed, scores, floor_score)
            highest = jnp.max(scores, axis=-1, keepdims=True)
            exp_terms = jnp.exp(scores - highest)
            if allowed is not None:
                exp_terms = jnp.where(allowed, exp_terms, 0.0)
            total = jnp.sum(exp_terms, axis=-1, keepdims=True)
            mixture = jnp.dot(
                exp_terms.astype(jnp.bfloat16), v2, preferred_element_type=jnp.float32
            )
            halves.append(mixture / total)
        attn_ref[:, cols] = jnp.where(low, halves[0], halves[1]).astype(jnp.bfloat16)
    if w_copies is not None:
        w_copies[3].wait()
    update = jnp.dot(attn_ref[...], wout_ref[...], preferred_element_type=jnp.float32)
    o_ref[...] = (rows + update).astype(jnp.bfloat16)
    if after_qkv is not None:
        for copy in after_qkv.copies[1:]:
            copy.wait()


class _Pair:
    def __init__(self, copies):
        self.copies = copies

    def start(self):
        for c in self.copies:
            c.start()

    def wait(self):
        for c in self.copies:
            c.wait()


def _no_mask(n_rows):
    return None


def _make_causal_mask(group):
    def mask_fn(n_rows):
        r_a = lax.broadcasted_iota(jnp.int32, (n_rows, n_rows), 0)
        r_b = lax.broadcasted_iota(jnp.int32, (n_rows, n_rows), 1)
        return (r_b <= r_a) & (jnp.bitwise_and(r_a - r_b, group - 1) == 0)

    return mask_fn


def _spatial_call(rows, qkv_weight, out_weight, next_qkv, next_out):
    n_rows, width = rows.shape

    def kernel(x_in, wqkv_hbm, wout_hbm, nqkv_hbm, nout_hbm, o_ref, nqkv_ref, nout_ref,
               x_vmem, wqkv_ref, wout_ref, packed_ref, attn_ref, sems):
        x_copy = pltpu.make_async_copy(x_in, x_vmem, sems.at[4])
        x_copy.start()
        w_copies = [
            pltpu.make_async_copy(
                wqkv_hbm.at[:, pl.ds(part * width, width)],
                wqkv_ref.at[:, pl.ds(part * width, width)],
                sems.at[part],
            )
            for part in range(3)
        ]
        w_copies.append(pltpu.make_async_copy(wout_hbm, wout_ref, sems.at[3]))
        for copy in w_copies[:3]:
            copy.start()
        after = _Pair([
            w_copies[3],
            pltpu.make_async_copy(nqkv_hbm, nqkv_ref, sems.at[5]),
            pltpu.make_async_copy(nout_hbm, nout_ref, sems.at[6]),
        ])
        x_copy.wait()
        _attention_block(
            x_vmem, w_copies, wqkv_ref, wout_ref, o_ref, packed_ref, attn_ref, _no_mask, after
        )

    vmem = pl.BlockSpec(memory_space=pltpu.VMEM)
    hbm = pl.BlockSpec(memory_space=pltpu.HBM)
    return pl.pallas_call(
        kernel,
        out_shape=(
            jax.ShapeDtypeStruct((n_rows, width), jnp.bfloat16),
            jax.ShapeDtypeStruct(next_qkv.shape, next_qkv.dtype),
            jax.ShapeDtypeStruct(next_out.shape, next_out.dtype),
        ),
        in_specs=[hbm] * 5,
        out_specs=(vmem, vmem, vmem),
        scratch_shapes=[
            pltpu.VMEM((n_rows, width), jnp.bfloat16),
            pltpu.VMEM((width, 3 * width), jnp.bfloat16),
            pltpu.VMEM((width, width), jnp.bfloat16),
            pltpu.VMEM((n_rows, 3 * width), jnp.bfloat16),
            pltpu.VMEM((n_rows, width), jnp.bfloat16),
            pltpu.SemaphoreType.DMA((7,)),
        ],
        compiler_params=pltpu.CompilerParams(vmem_limit_bytes=48 * 1024 * 1024),
    )(*[pltpu.with_memory_space_constraint(a, pltpu.HBM) for a in (rows, qkv_weight, out_weight, next_qkv, next_out)])


def _temporal_call(rows, qkv_weight, out_weight, mask_fn):
    n_rows, width = rows.shape

    def kernel(x_in, wqkv_in, wout_in, o_ref, packed_ref, attn_ref):
        _attention_block(x_in, None, wqkv_in, wout_in, o_ref, packed_ref, attn_ref, mask_fn)

    vmem = pl.BlockSpec(memory_space=pltpu.VMEM)
    return pl.pallas_call(
        kernel,
        out_shape=jax.ShapeDtypeStruct((n_rows, width), jnp.bfloat16),
        in_specs=[vmem, vmem, vmem],
        out_specs=vmem,
        scratch_shapes=[
            pltpu.VMEM((n_rows, 3 * width), jnp.bfloat16),
            pltpu.VMEM((n_rows, width), jnp.bfloat16),
        ],
        compiler_params=pltpu.CompilerParams(vmem_limit_bytes=48 * 1024 * 1024),
    )(rows, qkv_weight, out_weight)


def body(frames_in, spatial_qkv, spatial_out, temporal_qkv, temporal_out):
    n_frames, n_patches, width = frames_in.shape
    assert n_frames == 1
    group = lax.axis_size(("patch", "tm"))
    hidden, t_qkv, t_out = _spatial_call(
        frames_in[0], spatial_qkv, spatial_out, temporal_qkv, temporal_out
    )
    columns = lax.all_to_all(
        hidden.reshape(group, n_patches // group, width),
        ("patch", "tm"),
        split_axis=0,
        concat_axis=0,
        tiled=True,
    )
    frame_total, column_count, _ = columns.shape
    assert column_count & (column_count - 1) == 0
    result = _temporal_call(
        columns.reshape(frame_total * column_count, width),
        t_qkv,
        t_out,
        _make_causal_mask(column_count),
    ).reshape(frame_total, column_count, width)
    return lax.all_to_all(result, ("patch", "tm"), split_axis=0, concat_axis=1, tiled=True)


def solution(mesh):
    in_specs = (P(("subject", "patch", "tm"), None, None), P(), P(), P(), P())
    out_specs = P(("subject", "patch", "tm"), None, None)
    return jax.shard_map(body, mesh=mesh, in_specs=in_specs, out_specs=out_specs, check_vma=False)
```
